256 devices in a mesh: wide: 64 (over y, z, core), col: 4 (over x).
Axes of the slice: x: 4, y: 4, z: 8, core: 2. Of those that a mesh axis runs over, the one named last changes fastest.
Arguments:
- assembled: float32 [9216, 1024], P(('wide', 'col')), as said below
- row_map: int32 [9216], P(('wide', 'col')), may hold values from 0 to 9215, as said below
- fill_pattern: int32 [2, 32], replicated, may hold values from 0 to 1
- trailing_block: float32 [64, 4, 32, 8192], P(None, 'col', None, 'wide'), may hold values from -6 to 6
Outputs:
- schur: float32 [64, 4, 32, 8192], P(None, 'col', None, 'wide')
- panel_rows: float32 [8192, 1024], P(('wide', 'col'))
- diag_factor: float32 [1024, 1024], P(('wide', 'col'))
The draws below stay inside these ranges and needn't reach their ends.
Inputs may be any that keep to these rules, and one draw needn't show every extreme that they name: row_map is a permutation of the window rows. Each device, with col index c, holds exactly 32 trailing rows 1024 + t whose owner device index t // 32 has col index c, and exactly 4 rows d below 1024 with d // 256 equal to c. At most 2 of one device's trailing rows have the same owner, and every device holds exactly 2 trailing rows of some owner. `assembled`: D is symmetric positive definite.
All inputs are finite; a program needn't handle non-finite values.
Results may differ from the reference program's by a relative error of at most 0.00008.
Values sent between devices are 32-bit elements; how exact they have to be, the bound alone decides.
No kernel may reach another device: no remote copies, remote signals or barrier semaphores. Data moves between devices by JAX's collectives and lax.ppermute only.
A program may use at most 128 MiB of HBM per device.

```python
import jax
import jax.numpy as jnp
from jax import lax

PANEL = 512
BLOCK = 256
TRAIL_DEV = 32
SLOT_CAP = 2
DIAG_DEV = 4
ASM_DEV = 36
TRAIL = 8192
BLOCKS = 32
N_WIDE = 64
N_COL = 4


def route_table(key):
    base_key = jax.random.fold_in(key, 7)
    class_keys = jax.random.split(base_key, N_COL)

    def one_class(class_key, column):
        keys = jax.random.split(class_key, 7)
        repeated = jnp.repeat(jnp.arange(N_WIDE), SLOT_CAP)
        chosen = jax.random.randint(keys[0], (), 0, N_WIDE)
        priority = jax.random.permutation(keys[1], N_WIDE * SLOT_CAP)
        priority = jnp.where(repeated == chosen, -1, priority)
        offsets = repeated[jnp.argsort(priority, stable=True)[:TRAIL_DEV]]
        source_label = jax.random.permutation(keys[2], N_WIDE)
        owner_label = jax.random.permutation(keys[3], N_WIDE)
        owners = owner_label[(source_label[:, None] + offsets[None, :]) % N_WIDE]
        flat_owner = owners.reshape(-1)
        onehot = (flat_owner[:, None] == jnp.arange(N_WIDE)[None, :]).astype(jnp.int32)
        before = jnp.cumsum(onehot, axis=0) - onehot
        position = jnp.sum(before * onehot, axis=1)
        local_orders = jax.vmap(lambda sub_key: jax.random.permutation(sub_key, TRAIL_DEV))(jax.random.split(keys[4], N_WIDE))
        local_rows = local_orders[flat_owner, position]
        trail_ids = 2 * PANEL + (flat_owner * N_COL + column) * TRAIL_DEV + local_rows
        trail_ids = trail_ids.reshape(N_WIDE, TRAIL_DEV)
        diag_count = 2 * PANEL // N_COL
        diag_ids = column * diag_count + jax.random.permutation(keys[5], diag_count)
        diag_ids = diag_ids.reshape(N_WIDE, DIAG_DEV)
        all_rows = jnp.concatenate([trail_ids, diag_ids], axis=1)
        shuffle = jax.vmap(lambda sub_key: jax.random.permutation(sub_key, ASM_DEV))(jax.random.split(keys[6], N_WIDE))
        return jnp.take_along_axis(all_rows, shuffle, axis=1)
    table = jax.vmap(one_class)(class_keys, jnp.arange(N_COL))
    return jnp.transpose(table, (1, 0, 2)).reshape(-1).astype(jnp.int32)


def draw_row_map(key, part):
    return route_table(key)


def draw_assembled(key, part):
    table = route_table(key)
    keys = jax.random.split(jax.random.fold_in(key, 11), 3)
    order_size = 2 * PANEL
    shape = (N_WIDE * N_COL * ASM_DEV, order_size)
    noise = jax.random.normal(keys[0], shape, jnp.float32)
    mixing = jax.random.normal(keys[1], (order_size, order_size), jnp.float32)
    lift = jax.random.uniform(keys[2], (order_size,), jnp.float32, 0.5, 1.5)
    gram = jnp.dot(mixing, mixing.T, precision=lax.Precision.HIGHEST) / order_size
    dense = gram + jnp.diag(lift)
    is_diagonal = table < order_size
    diag_ids = jnp.clip(table, 0, order_size - 1)
    diag_part = dense[diag_ids]
    trail_part = 0.1 * noise
    return jnp.where(is_diagonal[:, None], diag_part, trail_part).astype(jnp.float32)


def draw_fill_pattern(key, part):
    keys = jax.random.split(jax.random.fold_in(key, 3), 2)
    first = jax.random.randint(keys[0], (BLOCKS,), 0, 2)
    extra = jax.random.randint(keys[1], (BLOCKS,), 0, 2)
    return jnp.stack([first, jnp.maximum(first, extra)]).astype(jnp.int32)


def block_scale(key, dims, cuts, smallest, top_value):
    level, own = 1.0, jax.random.fold_in(key, 6)
    for dim, blocks in cuts:
        steps = jnp.exp(jax.random.uniform(jax.random.fold_in(own, dim), (blocks,), jnp.float32, smallest / len(cuts), top_value / len(cuts)))
        level = level * jnp.repeat(steps, dims[dim] // blocks).reshape([-1 if axis == dim else 1 for axis in range(len(dims))])
    return level


def centred(key, shape, deviation, most, cuts=(), kind=jnp.bfloat16):
    array = jax.random.normal(key, shape, jnp.float32) * deviation
    if len(cuts) > 0:
        array = block_scale(key, shape, cuts, -0.22, 0.18) * array
    return jnp.clip(array, min=-most, max=most).astype(kind)


def setup_inputs(seed: int = 0) -> dict:
    arg_keys = jax.random.split(jax.random.key(seed), 5)
    assembled = draw_assembled(jax.random.fold_in(arg_keys[4], 71), 0)
    row_map = draw_row_map(jax.random.fold_in(arg_keys[4], 71), 0)
    fill_pattern = draw_fill_pattern(jax.random.fold_in(arg_keys[4], 71), 0)
    trailing_block = centred(arg_keys[3], (N_WIDE, N_COL, TRAIL_DEV, TRAIL), 1.0, 6.0, ((1, 4), (3, 64)), jnp.float32)
    return dict(assembled=assembled, row_map=row_map, fill_pattern=fill_pattern, trailing_block=trailing_block)


highest = lax.Precision.HIGHEST

def lower_inverse(lower_factor):
    order_size = lower_factor.shape[0]
    identity = jnp.eye(order_size, dtype=lower_factor.dtype)
    return lax.linalg.triangular_solve(lower_factor, identity, left_side=True, lower=True)

def contract_rows(left_rows, right_rows):
    return lax.dot_general(left_rows, right_rows, (((1,), (1,)), ((), ())), precision=highest)

def reference(assembled, row_map, fill_pattern, trailing_block):
    twice_width = 2 * PANEL
    placed = jnp.zeros((twice_width + TRAIL, twice_width), assembled.dtype).at[row_map].set(assembled)
    gathered = placed[:twice_width]
    symmetric = (gathered + gathered.T) * 0.5
    diag_factor = jnp.linalg.cholesky(symmetric)
    inverse = lower_inverse(diag_factor)
    block_ids = jnp.arange(TRAIL) // BLOCK
    first_flags = fill_pattern[0][block_ids]
    second_flags = fill_pattern[1][block_ids]
    column_first = jnp.arange(twice_width) < PANEL
    keep = jnp.where(column_first[None, :], first_flags[:, None], second_flags[:, None]).astype(assembled.dtype)
    masked = placed[twice_width:] * keep
    panel_rows = contract_rows(masked, inverse)
    whole = trailing_block.reshape(TRAIL, TRAIL)
    schur = (whole - contract_rows(panel_rows, panel_rows)).reshape(trailing_block.shape)
    return (schur, panel_rows, diag_factor)
```

```python
import jax
import jax.numpy as jnp
from jax import lax
from jax.sharding import PartitionSpec as P

BLOCK = 256

highest = lax.Precision.HIGHEST


def lower_inverse(lower_factor):
    order_size = lower_factor.shape[0]
    identity = jnp.eye(order_size, dtype=lower_factor.dtype)
    return lax.linalg.triangular_solve(lower_factor, identity, left_side=True, lower=True)


def contract_rows(left_rows, right_rows):
    return lax.dot_general(left_rows, right_rows, (((1,), (1,)), ((), ())), precision=highest)


def local(assembled, row_map, fill_pattern, trailing_block):
    wide_count = lax.axis_size("wide")
    col_count = lax.axis_size("col")
    asm_rows, twice_width = assembled.shape
    half_width = twice_width // 2
    trail_rows = trailing_block.shape[2]
    diag_share = twice_width // (col_count * wide_count)
    diag_col = twice_width // col_count
    wide_index = lax.axis_index("wide")
    col_index = lax.axis_index("col")
    device_index = wide_index * col_count + col_index

    packed_rows = ((asm_rows + 1 + 7) // 8) * 8
    id_row = jnp.zeros((twice_width,), jnp.float32).at[:asm_rows].set(row_map.astype(jnp.float32))
    packed = jnp.concatenate(
        [assembled, id_row[None, :], jnp.zeros((packed_rows - asm_rows - 1, twice_width), jnp.float32)],
        axis=0,
    )
    gathered = lax.all_gather(packed, "wide", axis=0, tiled=True)
    gathered3 = gathered.reshape(wide_count, packed_rows, twice_width)
    ids = gathered3[:, asm_rows, :asm_rows].astype(jnp.int32).reshape(-1)
    source = (
        jnp.arange(wide_count)[:, None] * packed_rows + jnp.arange(asm_rows)[None, :]
    ).reshape(-1)

    is_diagonal = ids < twice_width
    diag_slot = jnp.where(is_diagonal, ids - diag_col * col_index, diag_col)
    diag_src = jnp.zeros((diag_col,), jnp.int32).at[diag_slot].set(source, mode="drop")
    diag_block = gathered[diag_src]
    full = lax.all_gather(diag_block, "col", axis=0, tiled=True)

    trail_id = ids - twice_width
    owner_wide = trail_id // (trail_rows * col_count)
    trail_slot = jnp.where(is_diagonal, wide_count * trail_rows, owner_wide * trail_rows + trail_id % trail_rows)
    trail_src = jnp.zeros((wide_count * trail_rows,), jnp.int32).at[trail_slot].set(source, mode="drop")
    trail_all = gathered[trail_src]
    row_global = (
        (jnp.arange(wide_count)[:, None] * col_count + col_index) * trail_rows
        + jnp.arange(trail_rows)[None, :]
    ).reshape(-1)
    block_ids = row_global // BLOCK
    first_flags = fill_pattern[0][block_ids]
    second_flags = fill_pattern[1][block_ids]
    column_first = jnp.arange(twice_width) < half_width
    keep = jnp.where(column_first[None, :], first_flags[:, None], second_flags[:, None]).astype(jnp.float32)
    masked_all = trail_all * keep
    masked_own = lax.dynamic_slice_in_dim(masked_all, wide_index * trail_rows, trail_rows, 0)
    masked_range = lax.all_gather(masked_own, "col", axis=0, tiled=True)

    symmetric = (full + full.T) * 0.5
    factor = jnp.linalg.cholesky(symmetric)
    inverse = lower_inverse(factor)
    panel = contract_rows(masked_own, inverse)
    range_panel = contract_rows(masked_range, inverse)
    range_back = lax.dot_general(range_panel, inverse, (((1,), (0,)), ((), ())), precision=highest)
    update = contract_rows(masked_all, range_back)
    schur = trailing_block - update.reshape(trailing_block.shape)
    factor_rows = lax.dynamic_slice_in_dim(factor, device_index * diag_share, diag_share, 0)
    return (schur, panel, factor_rows)


def solution(mesh):
    in_specs = (P(("wide", "col"), None), P(("wide", "col")), P(), P(None, "col", None, "wide"))
    out_specs = (P(None, "col", None, "wide"), P(("wide", "col"), None), P(("wide", "col"), None))
    return jax.shard_map(local, mesh=mesh, in_specs=in_specs, out_specs=out_specs, check_vma=False)
```

```python
import jax
import jax.numpy as jnp
from jax import lax
from jax.sharding import PartitionSpec as P

BLOCK = 256
FACTOR_BLOCK = 128

highest = lax.Precision.HIGHEST


def lower_inverse(lower_factor):
    order_size = lower_factor.shape[0]
    identity = jnp.eye(order_size, dtype=lower_factor.dtype)
    return lax.linalg.triangular_solve(lower_factor, identity, left_side=True, lower=True)


def contract_rows(left_rows, right_rows):
    return lax.dot_general(left_rows, right_rows, (((1,), (1,)), ((), ())), precision=highest)


def matmul(left, right):
    return lax.dot_general(left, right, (((1,), (0,)), ((), ())), precision=highest)


def factor_and_inverse(gathered):
    order_size = gathered.shape[0]
    size = FACTOR_BLOCK
    count = order_size // size
    factor = jnp.zeros((order_size, order_size), jnp.float32)
    diag_inverses = []
    for k in range(count):
        start = k * size
        column = (gathered[start:, start:start + size] + gathered[start:start + size, start:].T) * 0.5
        if k > 0:
            column = column - contract_rows(factor[start:, :start], factor[start:start + size, :start])
        block = jnp.tril(lax.linalg.cholesky(column[:size], symmetrize_input=False))
        block_inverse = jnp.tril(lower_inverse(block))
        factor = factor.at[start:start + size, start:start + size].set(block)
        if k < count - 1:
            factor = factor.at[start + size:, start:start + size].set(contract_rows(column[size:], block_inverse))
        diag_inverses.append(block_inverse)
    inverse = jnp.zeros((order_size, order_size), jnp.float32)
    inverse = inverse.at[:size, :size].set(diag_inverses[0])
    for k in range(1, count):
        start = k * size
        partial = matmul(factor[start:start + size, :start], inverse[:start, :start])
        inverse = inverse.at[start:start + size, :start].set(-matmul(diag_inverses[k], partial))
        inverse = inverse.at[start:start + size, start:start + size].set(diag_inverses[k])
    return factor, inverse


def local(assembled, row_map, fill_pattern, trailing_block):
    wide_count = lax.axis_size("wide")
    col_count = lax.axis_size("col")
    asm_rows, twice_width = assembled.shape
    half_width = twice_width // 2
    trail_rows = trailing_block.shape[2]
    blocks = fill_pattern.shape[1]
    diag_share = twice_width // (col_count * wide_count)
    diag_col = twice_width // col_count
    trail_col = wide_count * trail_rows
    wide_index = lax.axis_index("wide")
    col_index = lax.axis_index("col")
    device_index = wide_index * col_count + col_index
    is_diagonal = row_map < twice_width

    order_ids = jnp.argsort(jnp.where(is_diagonal, 0, 1), stable=True)[:diag_share]
    diag_pack_rows = ((diag_share + 1 + 7) // 8) * 8
    diag_id_row = jnp.zeros((twice_width,), jnp.float32).at[:diag_share].set(row_map[order_ids].astype(jnp.float32))
    diag_pack = jnp.concatenate(
        [assembled[order_ids], diag_id_row[None, :],
         jnp.zeros((diag_pack_rows - diag_share - 1, twice_width), jnp.float32)], axis=0)
    diag_wide = lax.all_gather(diag_pack, "wide", axis=0, tiled=True).reshape(wide_count, diag_pack_rows, twice_width)
    diag_rows = diag_wide[:, :diag_share, :].reshape(wide_count * diag_share, twice_width)
    diag_slot = diag_wide[:, diag_share, :diag_share].astype(jnp.int32).reshape(-1) - diag_col * col_index
    diag_block = jnp.zeros((diag_col, twice_width), jnp.float32).at[diag_slot].set(diag_rows, mode="drop")
    full = lax.all_gather(diag_block, "col", axis=0, tiled=True)

    packed_rows = ((asm_rows + 1 + 7) // 8) * 8
    id_row = jnp.zeros((twice_width,), jnp.float32).at[:asm_rows].set(row_map.astype(jnp.float32))
    packed = jnp.concatenate(
        [assembled, id_row[None, :], jnp.zeros((packed_rows - asm_rows - 1, twice_width), jnp.float32)], axis=0)
    packed, full = lax.optimization_barrier((packed, full))
    gathered = lax.all_gather(packed, "wide", axis=0, tiled=True)
    gathered3 = gathered.reshape(wide_count, packed_rows, twice_width)
    ids = gathered3[:, asm_rows, :asm_rows].astype(jnp.int32)
    trail_id = ids - twice_width
    trail_slot = (trail_id // (trail_rows * col_count)) * trail_rows + trail_id % trail_rows
    key = jnp.where(ids >= twice_width, trail_slot, trail_col)
    key = jnp.concatenate([key, jnp.full((wide_count, packed_rows - asm_rows), trail_col, jnp.int32)], axis=1)
    key = key.reshape(-1)
    _, order = lax.sort((key, jnp.arange(key.shape[0], dtype=jnp.int32)), num_keys=1)
    trail_src = order[:trail_col]

    block_of = jnp.concatenate(
        [trail_id // BLOCK, jnp.full((wide_count, packed_rows - asm_rows), -1, jnp.int32)], axis=1).reshape(-1)
    block_hits = (block_of[:, None] == jnp.arange(blocks)[None, :]).astype(jnp.int32)
    first_keep = jnp.sum(block_hits * fill_pattern[0][None, :], axis=1).astype(jnp.float32)
    second_keep = jnp.sum(block_hits * fill_pattern[1][None, :], axis=1).astype(jnp.float32)

    own_src = lax.dynamic_slice_in_dim(trail_src, wide_index * trail_rows, trail_rows, 0)
    column_first = jnp.arange(twice_width) < half_width
    own_keep = jnp.where(column_first[None, :], first_keep[own_src][:, None], second_keep[own_src][:, None])
    masked_own = gathered[own_src] * own_keep
    masked_range = lax.all_gather(masked_own, "col", axis=0, tiled=True)

    factor, inverse = factor_and_inverse(full)
    range_panel = contract_rows(masked_range, inverse)
    panel = lax.dynamic_slice_in_dim(range_panel, col_index * trail_rows, trail_rows, 0)
    range_back = matmul(range_panel, inverse)
    first_part = contract_rows(gathered[:, :half_width], range_back[:, :half_width])
    second_part = contract_rows(gathered[:, half_width:], range_back[:, half_width:])
    update_all = first_keep[:, None] * first_part + second_keep[:, None] * second_part
    update = update_all[trail_src]
    schur = trailing_block - update.reshape(trailing_block.shape)
    factor_rows = lax.dynamic_slice_in_dim(factor, device_index * diag_share, diag_share, 0)
    return (schur, panel, factor_rows)


def solution(mesh):
    in_specs = (P(("wide", "col"), None), P(("wide", "col")), P(), P(None, "col", None, "wide"))
    out_specs = (P(None, "col", None, "wide"), P(("wide", "col"), None), P(("wide", "col"), None))
    return jax.shard_map(local, mesh=mesh, in_specs=in_specs, out_specs=out_specs, check_vma=False)
```

```python
import jax
import jax.numpy as jnp
from jax import lax
from jax.sharding import PartitionSpec as P

BLOCK = 256
LANE_PAD = 128
WIDE_PARTS = ("y", "z", "core")
FACTOR_BLOCK = 128

highest = lax.Precision.HIGHEST


def lower_inverse(lower_factor):
    order_size = lower_factor.shape[0]
    identity = jnp.eye(order_size, dtype=lower_factor.dtype)
    return lax.linalg.triangular_solve(lower_factor, identity, left_side=True, lower=True)


def contract_rows(left_rows, right_rows):
    return lax.dot_general(left_rows, right_rows, (((1,), (1,)), ((), ())), precision=highest)


def matmul(left, right):
    return lax.dot_general(left, right, (((1,), (0,)), ((), ())), precision=highest)


def factor_and_inverse(gathered, tied, exchange):
    order_size = gathered.shape[0]
    size = FACTOR_BLOCK
    count = order_size // size
    factor = jnp.zeros((order_size, order_size), jnp.float32)
    diag_inverses = []
    for k in range(count):
        start = k * size
        column = (gathered[start:, start:start + size] + gathered[start:start + size, start:].T) * 0.5
        if k > 0:
            column = column - contract_rows(factor[start:, :start], factor[start:start + size, :start])
        block = jnp.tril(lax.linalg.cholesky(column[:size], symmetrize_input=False))
        block_inverse = jnp.tril(lower_inverse(block))
        factor = factor.at[start:start + size, start:start + size].set(block)
        if k < count - 1:
            factor = factor.at[start + size:, start:start + size].set(contract_rows(column[size:], block_inverse))
        diag_inverses.append(block_inverse)
        if k == count // 2:
            factor, tied = lax.optimization_barrier((factor, tied))
            tied = exchange(tied)
    inverse = jnp.zeros((order_size, order_size), jnp.float32)
    inverse = inverse.at[:size, :size].set(diag_inverses[0])
    for k in range(1, count):
        start = k * size
        partial = matmul(factor[start:start + size, :start], inverse[:start, :start])
        inverse = inverse.at[start:start + size, :start].set(-matmul(diag_inverses[k], partial))
        inverse = inverse.at[start:start + size, start:start + size].set(diag_inverses[k])
    return factor, inverse, tied


def local(assembled, row_map, fill_pattern, trailing_block):
    wide_count = lax.axis_size(WIDE_PARTS)
    col_count = lax.axis_size("col")
    asm_rows, twice_width = assembled.shape
    half_width = twice_width // 2
    trail_rows = trailing_block.shape[2]
    blocks = fill_pattern.shape[1]
    diag_share = twice_width // (col_count * wide_count)
    diag_col = twice_width // col_count
    trail_col = wide_count * trail_rows
    wide_index = lax.axis_index(WIDE_PARTS)
    col_index = lax.axis_index("col")
    device_index = wide_index * col_count + col_index
    is_diagonal = row_map < twice_width

    order_ids = jnp.argsort(jnp.where(is_diagonal, 0, 1), stable=True)[:diag_share]
    diag_ids = row_map[order_ids].astype(jnp.float32)
    diag_pack = jnp.concatenate(
        [assembled[order_ids], jnp.broadcast_to(diag_ids[:, None], (diag_share, LANE_PAD))], axis=1)
    for axis in WIDE_PARTS[::-1]:
        diag_pack = lax.all_gather(diag_pack, axis, axis=0, tiled=True)
    diag_slot = diag_pack[:, twice_width].astype(jnp.int32) - diag_col * col_index
    diag_block = jnp.zeros((diag_col, twice_width), jnp.float32).at[diag_slot].set(
        diag_pack[:, :twice_width], mode="drop")
    full = lax.all_gather(diag_block, "col", axis=0, tiled=True)

    packed_rows = ((asm_rows + 1 + 7) // 8) * 8
    id_row = jnp.zeros((twice_width,), jnp.float32).at[:asm_rows].set(row_map.astype(jnp.float32))
    packed = jnp.concatenate(
        [assembled, id_row[None, :], jnp.zeros((packed_rows - asm_rows - 1, twice_width), jnp.float32)], axis=0)
    packed, full = lax.optimization_barrier((packed, full))
    gathered = lax.all_gather(packed, WIDE_PARTS, axis=0, tiled=True)
    gathered3 = gathered.reshape(wide_count, packed_rows, twice_width)
    ids = gathered3[:, asm_rows, :asm_rows].astype(jnp.int32)
    trail_id = ids - twice_width
    trail_slot = (trail_id // (trail_rows * col_count)) * trail_rows + trail_id % trail_rows
    key = jnp.where(ids >= twice_width, trail_slot, trail_col)
    key = jnp.concatenate([key, jnp.full((wide_count, packed_rows - asm_rows), trail_col, jnp.int32)], axis=1)
    key = key.reshape(-1)
    _, order = lax.sort((key, jnp.arange(key.shape[0], dtype=jnp.int32)), num_keys=1)
    trail_src = order[:trail_col]

    block_of = jnp.concatenate(
        [trail_id // BLOCK, jnp.full((wide_count, packed_rows - asm_rows), -1, jnp.int32)], axis=1).reshape(-1)
    block_hits = (block_of[:, None] == jnp.arange(blocks)[None, :]).astype(jnp.int32)
    first_keep = jnp.sum(block_hits * fill_pattern[0][None, :], axis=1).astype(jnp.float32)
    second_keep = jnp.sum(block_hits * fill_pattern[1][None, :], axis=1).astype(jnp.float32)

    own_src = lax.dynamic_slice_in_dim(trail_src, wide_index * trail_rows, trail_rows, 0)
    column_first = jnp.arange(twice_width) < half_width
    own_keep = jnp.where(column_first[None, :], first_keep[own_src][:, None], second_keep[own_src][:, None])
    masked_own = gathered[own_src] * own_keep
    placed_own = jnp.zeros((col_count * trail_rows, twice_width), jnp.float32)
    placed_own = lax.dynamic_update_slice_in_dim(placed_own, masked_own, col_index * trail_rows, 0)

    def exchange(tied):
        placed, first, second, source = tied
        return (lax.psum(placed, "col"), first, second, source)

    factor, inverse, tied = factor_and_inverse(full, (placed_own, first_keep, second_keep, trail_src), exchange)
    masked_range, first_keep, second_keep, trail_src = tied
    range_panel = contract_rows(masked_range, inverse)
    panel = lax.dynamic_slice_in_dim(range_panel, col_index * trail_rows, trail_rows, 0)
    range_back = matmul(range_panel, inverse)
    first_part = contract_rows(gathered[:, :half_width], range_back[:, :half_width])
    second_part = contract_rows(gathered[:, half_width:], range_back[:, half_width:])
    update_all = first_keep[:, None] * first_part + second_keep[:, None] * second_part
    update = update_all[trail_src]
    schur = trailing_block - update.reshape(trailing_block.shape)
    factor_rows = lax.dynamic_slice_in_dim(factor, device_index * diag_share, diag_share, 0)
    return (schur, panel, factor_rows)


def solution(mesh):
    wide_sizes = (4, 8, 2)
    split = jax.sharding.Mesh(
        mesh.devices.reshape(wide_sizes + (mesh.shape["col"],)), WIDE_PARTS + ("col",))
    rows = WIDE_PARTS + ("col",)
    in_specs = (P(rows, None), P(rows), P(), P(None, "col", None, WIDE_PARTS))
    out_specs = (P(None, "col", None, WIDE_PARTS), P(rows, None), P(rows, None))
    return jax.shard_map(local, mesh=split, in_specs=in_specs, out_specs=out_specs, check_vma=False)
```

```python
import jax
import jax.numpy as jnp
from jax import lax
from jax.sharding import PartitionSpec as P

BLOCK = 256
LANE_PAD = 128
WIDE_PARTS = ("y", "z", "core")
FACTOR_BLOCK = 128

highest = lax.Precision.HIGHEST


def lower_inverse(lower_factor):
    order_size = lower_factor.shape[0]
    identity = jnp.eye(order_size, dtype=lower_factor.dtype)
    return lax.linalg.triangular_solve(lower_factor, identity, left_side=True, lower=True)


def contract_rows(left_rows, right_rows):
    return lax.dot_general(left_rows, right_rows, (((1,), (1,)), ((), ())), precision=highest)


def matmul(left, right):
    return lax.dot_general(left, right, (((1,), (0,)), ((), ())), precision=highest)


def factor_and_inverse(gathered, tied, exchange):
    order_size = gathered.shape[0]
    size = FACTOR_BLOCK
    count = order_size // size
    factor = jnp.zeros((order_size, order_size), jnp.float32)
    diag_inverses = []
    for k in range(count):
        start = k * size
        column = (gathered[start:, start:start + size] + gathered[start:start + size, start:].T) * 0.5
        if k > 0:
            column = column - contract_rows(factor[start:, :start], factor[start:start + size, :start])
        block = jnp.tril(lax.linalg.cholesky(column[:size], symmetrize_input=False))
        block_inverse = jnp.tril(lower_inverse(block))
        factor = factor.at[start:start + size, start:start + size].set(block)
        if k < count - 1:
            factor = factor.at[start + size:, start:start + size].set(contract_rows(column[size:], block_inverse))
        diag_inverses.append(block_inverse)
        if k == count // 2:
            factor, tied = lax.optimization_barrier((factor, tied))
            tied = exchange(tied)
    inverse = jnp.zeros((order_size, order_size), jnp.float32)
    inverse = inverse.at[:size, :size].set(diag_inverses[0])
    for k in range(1, count):
        start = k * size
        partial = matmul(factor[start:start + size, :start], inverse[:start, :start])
        inverse = inverse.at[start:start + size, :start].set(-matmul(diag_inverses[k], partial))
        inverse = inverse.at[start:start + size, start:start + size].set(diag_inverses[k])
    return factor, inverse, tied


def local(assembled, row_map, fill_pattern, trailing_block):
    wide_count = lax.axis_size(WIDE_PARTS)
    col_count = lax.axis_size("col")
    asm_rows, twice_width = assembled.shape
    half_width = twice_width // 2
    trail_rows = trailing_block.shape[2]
    blocks = fill_pattern.shape[1]
    diag_share = twice_width // (col_count * wide_count)
    diag_col = twice_width // col_count
    trail_col = wide_count * trail_rows
    wide_index = lax.axis_index(WIDE_PARTS)
    col_index = lax.axis_index("col")
    device_index = wide_index * col_count + col_index
    is_diagonal = row_map < twice_width

    order_ids = jnp.argsort(jnp.where(is_diagonal, 0, 1), stable=True)[:diag_share]
    diag_ids = row_map[order_ids].astype(jnp.float32)
    diag_pack = jnp.concatenate(
        [assembled[order_ids], jnp.broadcast_to(diag_ids[:, None], (diag_share, LANE_PAD))], axis=1)
    for axis in WIDE_PARTS[::-1]:
        diag_pack = lax.all_gather(diag_pack, axis, axis=0, tiled=True)
    diag_slot = diag_pack[:, twice_width].astype(jnp.int32) - diag_col * col_index
    diag_block = jnp.zeros((diag_col, twice_width), jnp.float32).at[diag_slot].set(
        diag_pack[:, :twice_width], mode="drop")
    full = lax.all_gather(diag_block, "col", axis=0, tiled=True)

    packed_rows = ((asm_rows + 1 + 7) // 8) * 8
    id_row = jnp.zeros((twice_width,), jnp.float32).at[:asm_rows].set(row_map.astype(jnp.float32))
    packed = jnp.concatenate(
        [assembled, id_row[None, :], jnp.zeros((packed_rows - asm_rows - 1, twice_width), jnp.float32)], axis=0)
    packed, full = lax.optimization_barrier((packed, full))
    gathered = lax.all_gather(packed, WIDE_PARTS, axis=0, tiled=True)
    gathered3 = gathered.reshape(wide_count, packed_rows, twice_width)
    ids = gathered3[:, asm_rows, :asm_rows].astype(jnp.int32)
    trail_id = ids - twice_width
    trail_slot = (trail_id // (trail_rows * col_count)) * trail_rows + trail_id % trail_rows
    key = jnp.where(ids >= twice_width, trail_slot, trail_col)
    key = jnp.concatenate([key, jnp.full((wide_count, packed_rows - asm_rows), trail_col, jnp.int32)], axis=1)
    key = key.reshape(-1)
    _, order = lax.sort((key, jnp.arange(key.shape[0], dtype=jnp.int32)), num_keys=1)
    trail_src = order[:trail_col]

    block_of = jnp.concatenate(
        [trail_id // BLOCK, jnp.full((wide_count, packed_rows - asm_rows), -1, jnp.int32)], axis=1).reshape(-1)
    block_hits = (block_of[:, None] == jnp.arange(blocks)[None, :]).astype(jnp.int32)
    first_keep = jnp.sum(block_hits * fill_pattern[0][None, :], axis=1).astype(jnp.float32)
    second_keep = jnp.sum(block_hits * fill_pattern[1][None, :], axis=1).astype(jnp.float32)

    own_src = lax.dynamic_slice_in_dim(trail_src, wide_index * trail_rows, trail_rows, 0)
    column_first = jnp.arange(twice_width) < half_width
    own_keep = jnp.where(column_first[None, :], first_keep[own_src][:, None], second_keep[own_src][:, None])
    masked_own = gathered[own_src] * own_keep
    def exchange(tied):
        own, first, second, source = tied
        return (lax.all_gather(own, "col", axis=0, tiled=True), first, second, source)

    factor, inverse, tied = factor_and_inverse(full, (masked_own, first_keep, second_keep, trail_src), exchange)
    masked_range, first_keep, second_keep, trail_src = tied
    range_panel = contract_rows(masked_range, inverse)
    panel = lax.dynamic_slice_in_dim(range_panel, col_index * trail_rows, trail_rows, 0)
    range_back = matmul(range_panel, inverse)
    first_part = contract_rows(gathered[:, :half_width], range_back[:, :half_width])
    second_part = contract_rows(gathered[:, half_width:], range_back[:, half_width:])
    update_all = first_keep[:, None] * first_part + second_keep[:, None] * second_part
    update = update_all[trail_src]
    schur = trailing_block - update.reshape(trailing_block.shape)
    factor_rows = lax.dynamic_slice_in_dim(factor, device_index * diag_share, diag_share, 0)
    return (schur, panel, factor_rows)


def solution(mesh):
    wide_sizes = (4, 8, 2)
    split = jax.sharding.Mesh(
        mesh.devices.reshape(wide_sizes + (mesh.shape["col"],)), WIDE_PARTS + ("col",))
    rows = WIDE_PARTS + ("col",)
    in_specs = (P(rows, None), P(rows), P(), P(None, "col", None, WIDE_PARTS))
    out_specs = (P(None, "col", None, WIDE_PARTS), P(rows, None), P(rows, None))
    return jax.shard_map(local, mesh=split, in_specs=in_specs, out_specs=out_specs, check_vma=False)
```

```python
import jax
import jax.numpy as jnp
from jax import lax
from jax.sharding import PartitionSpec as P

BLOCK = 256
LANE_PAD = 128
WIDE_PARTS = ("y", "z", "core")
FACTOR_BLOCK = 128

highest = lax.Precision.HIGHEST


def lower_inverse(lower_factor):
    order_size = lower_factor.shape[0]
    identity = jnp.eye(order_size, dtype=lower_factor.dtype)
    return lax.linalg.triangular_solve(lower_factor, identity, left_side=True, lower=True)


def contract_rows(left_rows, right_rows):
    return lax.dot_general(left_rows, right_rows, (((1,), (1,)), ((), ())), precision=highest)


def matmul(left, right):
    return lax.dot_general(left, right, (((1,), (0,)), ((), ())), precision=highest)


def factor_and_inverse(gathered, tied, exchange):
    order_size = gathered.shape[0]
    size = FACTOR_BLOCK
    count = order_size // size
    factor = jnp.zeros((order_size, order_size), jnp.float32)
    diag_inverses = []
    for k in range(count):
        start = k * size
        column = (gathered[start:, start:start + size] + gathered[start:start + size, start:].T) * 0.5
        if k > 0:
            column = column - contract_rows(factor[start:, :start], factor[start:start + size, :start])
        block = jnp.tril(lax.linalg.cholesky(column[:size], symmetrize_input=False))
        block_inverse = jnp.tril(lower_inverse(block))
        factor = factor.at[start:start + size, start:start + size].set(block)
        if k < count - 1:
            factor = factor.at[start + size:, start:start + size].set(contract_rows(column[size:], block_inverse))
        diag_inverses.append(block_inverse)
        if k == count // 2:
            factor, tied = lax.optimization_barrier((factor, tied))
            tied = exchange(tied)
    inverse = jnp.zeros((order_size, order_size), jnp.float32)
    inverse = inverse.at[:size, :size].set(diag_inverses[0])
    for k in range(1, count):
        start = k * size
        partial = matmul(factor[start:start + size, :start], inverse[:start, :start])
        inverse = inverse.at[start:start + size, :start].set(-matmul(diag_inverses[k], partial))
        inverse = inverse.at[start:start + size, start:start + size].set(diag_inverses[k])
    return factor, inverse, tied


def local(assembled, row_map, fill_pattern, trailing_block):
    wide_count = lax.axis_size(WIDE_PARTS)
    col_count = lax.axis_size("col")
    asm_rows, twice_width = assembled.shape
    half_width = twice_width // 2
    trail_rows = trailing_block.shape[2]
    blocks = fill_pattern.shape[1]
    diag_share = twice_width // (col_count * wide_count)
    diag_col = twice_width // col_count
    trail_col = wide_count * trail_rows
    wide_index = lax.axis_index(WIDE_PARTS)
    col_index = lax.axis_index("col")
    device_index = wide_index * col_count + col_index
    is_diagonal = row_map < twice_width

    order_ids = jnp.argsort(jnp.where(is_diagonal, 0, 1), stable=True)[:diag_share]
    diag_ids = row_map[order_ids].astype(jnp.float32)
    diag_pack = jnp.concatenate(
        [assembled[order_ids], jnp.broadcast_to(diag_ids[:, None], (diag_share, LANE_PAD))], axis=1)
    for axis in ("core", "z", ("y", "col")):
        diag_pack = lax.all_gather(diag_pack, axis, axis=0, tiled=True)
    diag_slot = diag_pack[:, twice_width].astype(jnp.int32)
    full = jnp.zeros((twice_width, twice_width), jnp.float32).at[diag_slot].set(
        diag_pack[:, :twice_width], mode="drop")

    packed_rows = ((asm_rows + 1 + 7) // 8) * 8
    id_row = jnp.zeros((twice_width,), jnp.float32).at[:asm_rows].set(row_map.astype(jnp.float32))
    packed = jnp.concatenate(
        [assembled, id_row[None, :], jnp.zeros((packed_rows - asm_rows - 1, twice_width), jnp.float32)], axis=0)
    packed, full = lax.optimization_barrier((packed, full))
    gathered = lax.all_gather(packed, WIDE_PARTS, axis=0, tiled=True)
    gathered3 = gathered.reshape(wide_count, packed_rows, twice_width)
    ids = gathered3[:, asm_rows, :asm_rows].astype(jnp.int32)
    trail_id = ids - twice_width
    trail_slot = (trail_id // (trail_rows * col_count)) * trail_rows + trail_id % trail_rows
    key = jnp.where(ids >= twice_width, trail_slot, trail_col)
    key = jnp.concatenate([key, jnp.full((wide_count, packed_rows - asm_rows), trail_col, jnp.int32)], axis=1)
    key = key.reshape(-1)
    _, order = lax.sort((key, jnp.arange(key.shape[0], dtype=jnp.int32)), num_keys=1)
    trail_src = order[:trail_col]

    block_of = jnp.concatenate(
        [trail_id // BLOCK, jnp.full((wide_count, packed_rows - asm_rows), -1, jnp.int32)], axis=1).reshape(-1)
    block_hits = (block_of[:, None] == jnp.arange(blocks)[None, :]).astype(jnp.int32)
    first_keep = jnp.sum(block_hits * fill_pattern[0][None, :], axis=1).astype(jnp.float32)
    second_keep = jnp.sum(block_hits * fill_pattern[1][None, :], axis=1).astype(jnp.float32)

    own_src = lax.dynamic_slice_in_dim(trail_src, wide_index * trail_rows, trail_rows, 0)
    column_first = jnp.arange(twice_width) < half_width
    own_keep = jnp.where(column_first[None, :], first_keep[own_src][:, None], second_keep[own_src][:, None])
    masked_own = gathered[own_src] * own_keep
    def exchange(tied):
        own, first, second, source = tied
        rows = own.shape[0]
        owners = jnp.zeros((col_count * rows, own.shape[1]), jnp.float32)
        owners = lax.dynamic_update_slice_in_dim(owners, own, col_index * rows, 0)
        for shift in range(1, col_count):
            pairs = [(c, (c + shift) % col_count) for c in range(col_count)]
            arrived = lax.ppermute(own, "col", pairs)
            owners = lax.dynamic_update_slice_in_dim(
                owners, arrived, ((col_index - shift) % col_count) * rows, 0)
        return (owners, first, second, source)

    factor, inverse, tied = factor_and_inverse(full, (masked_own, first_keep, second_keep, trail_src), exchange)
    masked_range, first_keep, second_keep, trail_src = tied
    range_panel = contract_rows(masked_range, inverse)
    panel = lax.dynamic_slice_in_dim(range_panel, col_index * trail_rows, trail_rows, 0)
    range_back = matmul(range_panel, inverse)
    first_part = contract_rows(gathered[:, :half_width], range_back[:, :half_width])
    second_part = contract_rows(gathered[:, half_width:], range_back[:, half_width:])
    update_all = first_keep[:, None] * first_part + second_keep[:, None] * second_part
    update = update_all[trail_src]
    schur = trailing_block - update.reshape(trailing_block.shape)
    factor_rows = lax.dynamic_slice_in_dim(factor, device_index * diag_share, diag_share, 0)
    return (schur, panel, factor_rows)


def solution(mesh):
    wide_sizes = (4, 8, 2)
    split = jax.sharding.Mesh(
        mesh.devices.reshape(wide_sizes + (mesh.shape["col"],)), WIDE_PARTS + ("col",))
    rows = WIDE_PARTS + ("col",)
    in_specs = (P(rows, None), P(rows), P(), P(None, "col", None, WIDE_PARTS))
    out_specs = (P(None, "col", None, WIDE_PARTS), P(rows, None), P(rows, None))
    return jax.shard_map(local, mesh=split, in_specs=in_specs, out_specs=out_specs, check_vma=False)
```

```python
import jax
import jax.numpy as jnp
from jax import lax
from jax.sharding import PartitionSpec as P

BLOCK = 256
LANE_PAD = 128
WIDE_PARTS = ("y", "z", "core")
FACTOR_BLOCK = 128

highest = lax.Precision.HIGHEST


def lower_inverse(lower_factor):
    order_size = lower_factor.shape[0]
    identity = jnp.eye(order_size, dtype=lower_factor.dtype)
    return lax.linalg.triangular_solve(lower_factor, identity, left_side=True, lower=True)


def contract_rows(left_rows, right_rows):
    return lax.dot_general(left_rows, right_rows, (((1,), (1,)), ((), ())), precision=highest)


def matmul(left, right):
    return lax.dot_general(left, right, (((1,), (0,)), ((), ())), precision=highest)


def factor_and_inverse(gathered, tied, exchange):
    order_size = gathered.shape[0]
    size = FACTOR_BLOCK
    count = order_size // size
    factor = jnp.zeros((order_size, order_size), jnp.float32)
    diag_inverses = []
    for k in range(count):
        start = k * size
        column = (gathered[start:, start:start + size] + gathered[start:start + size, start:].T) * 0.5
        if k > 0:
            column = column - contract_rows(factor[start:, :start], factor[start:start + size, :start])
        block = jnp.tril(lax.linalg.cholesky(column[:size], symmetrize_input=False))
        block_inverse = jnp.tril(lower_inverse(block))
        factor = factor.at[start:start + size, start:start + size].set(block)
        if k < count - 1:
            factor = factor.at[start + size:, start:start + size].set(contract_rows(column[size:], block_inverse))
        diag_inverses.append(block_inverse)
        if k == count // 2:
            factor, tied = lax.optimization_barrier((factor, tied))
            tied = exchange(tied)
    inverse = jnp.zeros((order_size, order_size), jnp.float32)
    inverse = inverse.at[:size, :size].set(diag_inverses[0])
    for k in range(1, count):
        start = k * size
        partial = matmul(factor[start:start + size, :start], inverse[:start, :start])
        inverse = inverse.at[start:start + size, :start].set(-matmul(diag_inverses[k], partial))
        inverse = inverse.at[start:start + size, start:start + size].set(diag_inverses[k])
    return factor, inverse, tied


def local(assembled, row_map, fill_pattern, trailing_block):
    wide_count = lax.axis_size(WIDE_PARTS)
    col_count = lax.axis_size("col")
    asm_rows, twice_width = assembled.shape
    half_width = twice_width // 2
    trail_rows = trailing_block.shape[2]
    blocks = fill_pattern.shape[1]
    diag_share = twice_width // (col_count * wide_count)
    diag_col = twice_width // col_count
    trail_col = wide_count * trail_rows
    wide_index = lax.axis_index(WIDE_PARTS)
    col_index = lax.axis_index("col")
    device_index = wide_index * col_count + col_index
    is_diagonal = row_map < twice_width

    order_ids = jnp.argsort(jnp.where(is_diagonal, 0, 1), stable=True)[:diag_share]
    diag_ids = row_map[order_ids].astype(jnp.float32)
    diag_pack = jnp.concatenate(
        [assembled[order_ids], jnp.broadcast_to(diag_ids[:, None], (diag_share, LANE_PAD))], axis=1)
    for axis in (("z", "core"), ("y", "col")):
        diag_pack = lax.all_gather(diag_pack, axis, axis=0, tiled=True)
    diag_slot = diag_pack[:, twice_width].astype(jnp.int32)
    full = jnp.zeros((twice_width, twice_width), jnp.float32).at[diag_slot].set(
        diag_pack[:, :twice_width], mode="drop")

    trail_order = jnp.argsort(jnp.where(is_diagonal, 1, 0), stable=True)[:asm_rows - diag_share]
    trail_ids = row_map[trail_order]
    packed = jnp.concatenate(
        [assembled[trail_order],
         jnp.broadcast_to(trail_ids.astype(jnp.float32)[:, None], (asm_rows - diag_share, LANE_PAD))], axis=1)
    packed, full = lax.optimization_barrier((packed, full))
    gathered = lax.all_gather(packed, WIDE_PARTS, axis=0, tiled=True)
    ids = gathered[:, twice_width].astype(jnp.int32)
    gathered = gathered[:, :twice_width]
    trail_id = ids - twice_width
    key = (trail_id // (trail_rows * col_count)) * trail_rows + trail_id % trail_rows
    _, order = lax.sort((key, jnp.arange(key.shape[0], dtype=jnp.int32)), num_keys=1)
    trail_src = order

    block_of = trail_id // BLOCK
    block_hits = (block_of[:, None] == jnp.arange(blocks)[None, :]).astype(jnp.int32)
    first_keep = jnp.sum(block_hits * fill_pattern[0][None, :], axis=1).astype(jnp.float32)
    second_keep = jnp.sum(block_hits * fill_pattern[1][None, :], axis=1).astype(jnp.float32)

    own_src = lax.dynamic_slice_in_dim(trail_src, wide_index * trail_rows, trail_rows, 0)
    column_first = jnp.arange(twice_width) < half_width
    own_keep = jnp.where(column_first[None, :], first_keep[own_src][:, None], second_keep[own_src][:, None])
    masked_own = gathered[own_src] * own_keep
    def exchange(tied):
        own, first, second, source = tied
        rows = own.shape[0]
        owners = jnp.zeros((col_count * rows, own.shape[1]), jnp.float32)
        owners = lax.dynamic_update_slice_in_dim(owners, own, col_index * rows, 0)
        for shift in range(1, col_count):
            pairs = [(c, (c + shift) % col_count) for c in range(col_count)]
            arrived = lax.ppermute(own, "col", pairs)
            owners = lax.dynamic_update_slice_in_dim(
                owners, arrived, ((col_index - shift) % col_count) * rows, 0)
        return (owners, first, second, source)

    factor, inverse, tied = factor_and_inverse(full, (masked_own, first_keep, second_keep, trail_src), exchange)
    masked_range, first_keep, second_keep, trail_src = tied
    range_panel = contract_rows(masked_range, inverse)
    panel = lax.dynamic_slice_in_dim(range_panel, col_index * trail_rows, trail_rows, 0)
    range_back = matmul(range_panel, inverse)
    first_part = contract_rows(gathered[:, :half_width], range_back[:, :half_width])
    second_part = contract_rows(gathered[:, half_width:], range_back[:, half_width:])
    update_all = first_keep[:, None] * first_part + second_keep[:, None] * second_part
    update = update_all[trail_src]
    schur = trailing_block - update.reshape(trailing_block.shape)
    factor_rows = lax.dynamic_slice_in_dim(factor, device_index * diag_share, diag_share, 0)
    return (schur, panel, factor_rows)


def solution(mesh):
    wide_sizes = (4, 8, 2)
    split = jax.sharding.Mesh(
        mesh.devices.reshape(wide_sizes + (mesh.shape["col"],)), WIDE_PARTS + ("col",))
    rows = WIDE_PARTS + ("col",)
    in_specs = (P(rows, None), P(rows), P(), P(None, "col", None, WIDE_PARTS))
    out_specs = (P(None, "col", None, WIDE_PARTS), P(rows, None), P(rows, None))
    return jax.shard_map(local, mesh=split, in_specs=in_specs, out_specs=out_specs, check_vma=False)
```

```python
import jax
import jax.numpy as jnp
from jax import lax
from jax.sharding import PartitionSpec as P

BLOCK = 256
LANE_PAD = 128
WIDE_PARTS = ("y", "z", "core")
FACTOR_BLOCK = 128

highest = lax.Precision.HIGHEST


def lower_inverse(lower_factor):
    order_size = lower_factor.shape[0]
    identity = jnp.eye(order_size, dtype=lower_factor.dtype)
    return lax.linalg.triangular_solve(lower_factor, identity, left_side=True, lower=True)


def contract_rows(left_rows, right_rows):
    return lax.dot_general(left_rows, right_rows, (((1,), (1,)), ((), ())), precision=highest)


def matmul(left, right):
    return lax.dot_general(left, right, (((1,), (0,)), ((), ())), precision=highest)


def factor_and_inverse(gathered, tied, exchange):
    order_size = gathered.shape[0]
    size = FACTOR_BLOCK
    count = order_size // size
    factor = jnp.zeros((order_size, order_size), jnp.float32)
    diag_inverses = []
    for k in range(count):
        start = k * size
        column = (gathered[start:, start:start + size] + gathered[start:start + size, start:].T) * 0.5
        if k > 0:
            column = column - contract_rows(factor[start:, :start], factor[start:start + size, :start])
        block = jnp.tril(lax.linalg.cholesky(column[:size], symmetrize_input=False))
        block_inverse = jnp.tril(lower_inverse(block))
        factor = factor.at[start:start + size, start:start + size].set(block)
        if k < count - 1:
            factor = factor.at[start + size:, start:start + size].set(contract_rows(column[size:], block_inverse))
        diag_inverses.append(block_inverse)
        if k == count // 2:
            factor, tied = lax.optimization_barrier((factor, tied))
            tied = exchange(tied)
    inverse = jnp.zeros((order_size, order_size), jnp.float32)
    inverse = inverse.at[:size, :size].set(diag_inverses[0])
    for k in range(1, count):
        start = k * size
        partial = matmul(factor[start:start + size, :start], inverse[:start, :start])
        inverse = inverse.at[start:start + size, :start].set(-matmul(diag_inverses[k], partial))
        inverse = inverse.at[start:start + size, start:start + size].set(diag_inverses[k])
    return factor, inverse, tied


def local(assembled, row_map, fill_pattern, trailing_block):
    wide_count = lax.axis_size(WIDE_PARTS)
    col_count = lax.axis_size("col")
    asm_rows, twice_width = assembled.shape
    half_width = twice_width // 2
    trail_rows = trailing_block.shape[2]
    blocks = fill_pattern.shape[1]
    diag_share = twice_width // (col_count * wide_count)
    diag_col = twice_width // col_count
    trail_col = wide_count * trail_rows
    wide_index = lax.axis_index(WIDE_PARTS)
    col_index = lax.axis_index("col")
    device_index = wide_index * col_count + col_index
    is_diagonal = row_map < twice_width

    order_ids = jnp.argsort(jnp.where(is_diagonal, 0, 1), stable=True)[:diag_share]
    diag_ids = row_map[order_ids].astype(jnp.float32)
    diag_pack = jnp.concatenate(
        [assembled[order_ids], jnp.broadcast_to(diag_ids[:, None], (diag_share, LANE_PAD))], axis=1)
    for axis in (("z", "core"), ("y", "col")):
        diag_pack = lax.all_gather(diag_pack, axis, axis=0, tiled=True)
    diag_slot = diag_pack[:, twice_width].astype(jnp.int32)
    full = jnp.zeros((twice_width, twice_width), jnp.float32).at[diag_slot].set(
        diag_pack[:, :twice_width], mode="drop")

    trail_order = jnp.argsort(jnp.where(is_diagonal, 1, 0), stable=True)[:asm_rows - diag_share]
    trail_ids = row_map[trail_order]
    packed = jnp.concatenate(
        [assembled[trail_order],
         jnp.broadcast_to(trail_ids.astype(jnp.float32)[:, None], (asm_rows - diag_share, LANE_PAD))], axis=1)
    packed, full = lax.optimization_barrier((packed, full))
    gathered = lax.all_gather(packed, WIDE_PARTS, axis=0, tiled=True)
    ids = gathered[:, twice_width].astype(jnp.int32)
    gathered = gathered[:, :twice_width]
    trail_id = ids - twice_width
    key = (trail_id // (trail_rows * col_count)) * trail_rows + trail_id % trail_rows
    _, order = lax.sort((key, jnp.arange(key.shape[0], dtype=jnp.int32)), num_keys=1)
    trail_src = order

    block_of = trail_id // BLOCK
    block_hits = (block_of[:, None] == jnp.arange(blocks)[None, :]).astype(jnp.int32)
    first_keep = jnp.sum(block_hits * fill_pattern[0][None, :], axis=1).astype(jnp.float32)
    second_keep = jnp.sum(block_hits * fill_pattern[1][None, :], axis=1).astype(jnp.float32)

    own_src = lax.dynamic_slice_in_dim(trail_src, wide_index * trail_rows, trail_rows, 0)
    column_first = jnp.arange(twice_width) < half_width
    own_keep = jnp.where(column_first[None, :], first_keep[own_src][:, None], second_keep[own_src][:, None])
    masked_own = gathered[own_src] * own_keep
    def exchange(tied):
        own, first, second, source = tied
        rows = own.shape[0]
        owners = jnp.zeros((col_count * rows, own.shape[1]), jnp.float32)
        owners = lax.dynamic_update_slice_in_dim(owners, own, col_index * rows, 0)
        for shift in range(1, col_count):
            pairs = [(c, (c + shift) % col_count) for c in range(col_count)]
            arrived = lax.ppermute(own, "col", pairs)
            owners = lax.dynamic_update_slice_in_dim(
                owners, arrived, ((col_index - shift) % col_count) * rows, 0)
        return (owners, first, second, source)

    factor, inverse, tied = factor_and_inverse(full, (masked_own, first_keep, second_keep, trail_src), exchange)
    masked_range, first_keep, second_keep, trail_src = tied
    range_panel = contract_rows(masked_range, inverse)
    panel = lax.dynamic_slice_in_dim(range_panel, col_index * trail_rows, trail_rows, 0)
    range_back = matmul(range_panel, inverse)
    first_part = lax.dot_general(gathered[:, :half_width], range_back[:, :half_width],
                                 (((1,), (1,)), ((), ())), precision=lax.Precision.HIGH)
    second_part = lax.dot_general(gathered[:, half_width:], range_back[:, half_width:],
                                  (((1,), (1,)), ((), ())), precision=lax.Precision.HIGH)
    update_all = first_keep[:, None] * first_part + second_keep[:, None] * second_part
    update = update_all[trail_src]
    schur = trailing_block - update.reshape(trailing_block.shape)
    factor_rows = lax.dynamic_slice_in_dim(factor, device_index * diag_share, diag_share, 0)
    return (schur, panel, factor_rows)


def solution(mesh):
    wide_sizes = (4, 8, 2)
    split = jax.sharding.Mesh(
        mesh.devices.reshape(wide_sizes + (mesh.shape["col"],)), WIDE_PARTS + ("col",))
    rows = WIDE_PARTS + ("col",)
    in_specs = (P(rows, None), P(rows), P(), P(None, "col", None, WIDE_PARTS))
    out_specs = (P(None, "col", None, WIDE_PARTS), P(rows, None), P(rows, None))
    return jax.shard_map(local, mesh=split, in_specs=in_specs, out_specs=out_specs, check_vma=False)
```

```python
import jax
import jax.numpy as jnp
from jax import lax
from jax.sharding import PartitionSpec as P

BLOCK = 256
LANE_PAD = 128
WIDE_PARTS = ("y", "z", "core")
FACTOR_BLOCK = 128

highest = lax.Precision.HIGHEST


def lower_inverse(lower_factor):
    order_size = lower_factor.shape[0]
    identity = jnp.eye(order_size, dtype=lower_factor.dtype)
    return lax.linalg.triangular_solve(lower_factor, identity, left_side=True, lower=True)


def contract_rows(left_rows, right_rows):
    return lax.dot_general(left_rows, right_rows, (((1,), (1,)), ((), ())), precision=highest)


def matmul(left, right):
    return lax.dot_general(left, right, (((1,), (0,)), ((), ())), precision=highest)


def factor_and_inverse(gathered, tied, exchange):
    order_size = gathered.shape[0]
    size = FACTOR_BLOCK
    count = order_size // size
    factor = jnp.zeros((order_size, order_size), jnp.float32)
    diag_inverses = []
    for k in range(count):
        start = k * size
        column = (gathered[start:, start:start + size] + gathered[start:start + size, start:].T) * 0.5
        if k > 0:
            column = column - contract_rows(factor[start:, :start], factor[start:start + size, :start])
        block = jnp.tril(lax.linalg.cholesky(column[:size], symmetrize_input=False))
        block_inverse = jnp.tril(lower_inverse(block))
        factor = factor.at[start:start + size, start:start + size].set(block)
        if k < count - 1:
            factor = factor.at[start + size:, start:start + size].set(contract_rows(column[size:], block_inverse))
        diag_inverses.append(block_inverse)
        if k == count // 2:
            factor, tied = lax.optimization_barrier((factor, tied))
            tied = exchange(tied)
    inverse = jnp.zeros((order_size, order_size), jnp.float32)
    inverse = inverse.at[:size, :size].set(diag_inverses[0])
    for k in range(1, count):
        start = k * size
        partial = matmul(factor[start:start + size, :start], inverse[:start, :start])
        inverse = inverse.at[start:start + size, :start].set(-matmul(diag_inverses[k], partial))
        inverse = inverse.at[start:start + size, start:start + size].set(diag_inverses[k])
    return factor, inverse, tied


def local(assembled, row_map, fill_pattern, trailing_block):
    wide_count = lax.axis_size(WIDE_PARTS)
    col_count = lax.axis_size("col")
    asm_rows, twice_width = assembled.shape
    half_width = twice_width // 2
    trail_rows = trailing_block.shape[2]
    blocks = fill_pattern.shape[1]
    diag_share = twice_width // (col_count * wide_count)
    diag_col = twice_width // col_count
    trail_col = wide_count * trail_rows
    wide_index = lax.axis_index(WIDE_PARTS)
    col_index = lax.axis_index("col")
    device_index = wide_index * col_count + col_index
    is_diagonal = row_map < twice_width

    order_ids = jnp.argsort(jnp.where(is_diagonal, 0, 1), stable=True)[:diag_share]
    diag_ids = row_map[order_ids].astype(jnp.float32)
    diag_pack = jnp.concatenate(
        [assembled[order_ids], jnp.broadcast_to(diag_ids[:, None], (diag_share, LANE_PAD))], axis=1)
    for axis in (("z", "core"), ("y", "col")):
        diag_pack = lax.all_gather(diag_pack, axis, axis=0, tiled=True)
    diag_slot = diag_pack[:, twice_width].astype(jnp.int32)
    full = jnp.zeros((twice_width, twice_width), jnp.float32).at[diag_slot].set(
        diag_pack[:, :twice_width], mode="drop")

    trail_order = jnp.argsort(jnp.where(is_diagonal, 1, 0), stable=True)[:asm_rows - diag_share]
    trail_ids = row_map[trail_order]
    packed = jnp.concatenate(
        [assembled[trail_order],
         jnp.broadcast_to(trail_ids.astype(jnp.float32)[:, None], (asm_rows - diag_share, LANE_PAD))], axis=1)
    packed, full = lax.optimization_barrier((packed, full))
    gathered = lax.all_gather(packed, WIDE_PARTS, axis=0, tiled=True)
    ids = gathered[:, twice_width].astype(jnp.int32)
    gathered = gathered[:, :twice_width]
    trail_id = ids - twice_width
    key = (trail_id // (trail_rows * col_count)) * trail_rows + trail_id % trail_rows
    _, order = lax.sort((key, jnp.arange(key.shape[0], dtype=jnp.int32)), num_keys=1)
    trail_src = order

    block_of = trail_id // BLOCK
    block_hits = (block_of[:, None] == jnp.arange(blocks)[None, :]).astype(jnp.int32)
    first_keep = jnp.sum(block_hits * fill_pattern[0][None, :], axis=1).astype(jnp.float32)
    second_keep = jnp.sum(block_hits * fill_pattern[1][None, :], axis=1).astype(jnp.float32)

    own_src = lax.dynamic_slice_in_dim(trail_src, wide_index * trail_rows, trail_rows, 0)
    column_first = jnp.arange(twice_width) < half_width
    own_keep = jnp.where(column_first[None, :], first_keep[own_src][:, None], second_keep[own_src][:, None])
    masked_own = gathered[own_src] * own_keep
    def exchange(tied):
        own, first, second, source = tied
        rows = own.shape[0]
        owners = jnp.zeros((col_count * rows, own.shape[1]), jnp.float32)
        owners = lax.dynamic_update_slice_in_dim(owners, own, col_index * rows, 0)
        for shift in range(1, col_count):
            pairs = [(c, (c + shift) % col_count) for c in range(col_count)]
            arrived = lax.ppermute(own, "col", pairs)
            owners = lax.dynamic_update_slice_in_dim(
                owners, arrived, ((col_index - shift) % col_count) * rows, 0)
        return (owners, first, second, source)

    factor, inverse, tied = factor_and_inverse(full, (masked_own, first_keep, second_keep, trail_src), exchange)
    masked_range, first_keep, second_keep, trail_src = tied
    range_panel = contract_rows(masked_range, inverse)
    panel = lax.dynamic_slice_in_dim(range_panel, col_index * trail_rows, trail_rows, 0)
    range_back = lax.dot_general(range_panel, inverse, (((1,), (0,)), ((), ())), precision=lax.Precision.HIGH)
    first_part = lax.dot_general(gathered[:, :half_width], range_back[:, :half_width],
                                 (((1,), (1,)), ((), ())), precision=lax.Precision.HIGH)
    second_part = lax.dot_general(gathered[:, half_width:], range_back[:, half_width:],
                                  (((1,), (1,)), ((), ())), precision=lax.Precision.HIGH)
    update_all = first_keep[:, None] * first_part + second_keep[:, None] * second_part
    update = update_all[trail_src]
    schur = trailing_block - update.reshape(trailing_block.shape)
    factor_rows = lax.dynamic_slice_in_dim(factor, device_index * diag_share, diag_share, 0)
    return (schur, panel, factor_rows)


def solution(mesh):
    wide_sizes = (4, 8, 2)
    split = jax.sharding.Mesh(
        mesh.devices.reshape(wide_sizes + (mesh.shape["col"],)), WIDE_PARTS + ("col",))
    rows = WIDE_PARTS + ("col",)
    in_specs = (P(rows, None), P(rows), P(), P(None, "col", None, WIDE_PARTS))
    out_specs = (P(None, "col", None, WIDE_PARTS), P(rows, None), P(rows, None))
    return jax.shard_map(local, mesh=split, in_specs=in_specs, out_specs=out_specs, check_vma=False)
```

```python
import jax
import jax.numpy as jnp
from jax import lax
from jax.sharding import PartitionSpec as P

BLOCK = 256
LANE_PAD = 128
WIDE_PARTS = ("y", "z", "core")
FACTOR_BLOCK = 128

highest = lax.Precision.HIGHEST


def lower_inverse(lower_factor):
    order_size = lower_factor.shape[0]
    identity = jnp.eye(order_size, dtype=lower_factor.dtype)
    return lax.linalg.triangular_solve(lower_factor, identity, left_side=True, lower=True)


def contract_rows(left_rows, right_rows):
    return lax.dot_general(left_rows, right_rows, (((1,), (1,)), ((), ())), precision=highest)


def matmul(left, right):
    return lax.dot_general(left, right, (((1,), (0,)), ((), ())), precision=highest)


def factor_and_inverse(gathered, tied, exchange):
    order_size = gathered.shape[0]
    size = FACTOR_BLOCK
    count = order_size // size
    factor = jnp.zeros((order_size, order_size), jnp.float32)
    diag_inverses = []
    for k in range(count):
        start = k * size
        end = start + size
        top = (gathered[start:end, start:end] + gathered[start:end, start:end].T) * 0.5
        if k > 0:
            top = top - contract_rows(factor[start:end, :start], factor[start:end, :start])
        block = jnp.tril(lax.linalg.cholesky(top, symmetrize_input=False))
        block_inverse = jnp.tril(lower_inverse(block))
        factor = factor.at[start:end, start:end].set(block)
        if k < count - 1:
            below = (gathered[end:, start:end] + gathered[start:end, end:].T) * 0.5
            if k > 0:
                below = below - contract_rows(factor[end:, :start], factor[start:end, :start])
            factor = factor.at[end:, start:end].set(contract_rows(below, block_inverse))
        diag_inverses.append(block_inverse)
        if k == count // 2:
            factor, tied = lax.optimization_barrier((factor, tied))
            tied = exchange(tied)
    inverse = jnp.zeros((order_size, order_size), jnp.float32)
    inverse = inverse.at[:size, :size].set(diag_inverses[0])
    for k in range(1, count):
        start = k * size
        partial = matmul(factor[start:start + size, :start], inverse[:start, :start])
        inverse = inverse.at[start:start + size, :start].set(-matmul(diag_inverses[k], partial))
        inverse = inverse.at[start:start + size, start:start + size].set(diag_inverses[k])
    return factor, inverse, tied


def local(assembled, row_map, fill_pattern, trailing_block):
    wide_count = lax.axis_size(WIDE_PARTS)
    col_count = lax.axis_size("col")
    asm_rows, twice_width = assembled.shape
    half_width = twice_width // 2
    trail_rows = trailing_block.shape[2]
    blocks = fill_pattern.shape[1]
    diag_share = twice_width // (col_count * wide_count)
    diag_col = twice_width // col_count
    trail_col = wide_count * trail_rows
    wide_index = lax.axis_index(WIDE_PARTS)
    col_index = lax.axis_index("col")
    device_index = wide_index * col_count + col_index
    is_diagonal = row_map < twice_width

    order_ids = jnp.argsort(jnp.where(is_diagonal, 0, 1), stable=True)[:diag_share]
    diag_ids = row_map[order_ids].astype(jnp.float32)
    diag_pack = jnp.concatenate(
        [assembled[order_ids], jnp.broadcast_to(diag_ids[:, None], (diag_share, LANE_PAD))], axis=1)
    for axis in (("z", "core"), ("y", "col")):
        diag_pack = lax.all_gather(diag_pack, axis, axis=0, tiled=True)
    diag_slot = diag_pack[:, twice_width].astype(jnp.int32)
    full = jnp.zeros((twice_width, twice_width), jnp.float32).at[diag_slot].set(
        diag_pack[:, :twice_width], mode="drop")

    trail_order = jnp.argsort(jnp.where(is_diagonal, 1, 0), stable=True)[:asm_rows - diag_share]
    trail_ids = row_map[trail_order]
    packed = jnp.concatenate(
        [assembled[trail_order],
         jnp.broadcast_to(trail_ids.astype(jnp.float32)[:, None], (asm_rows - diag_share, LANE_PAD))], axis=1)
    packed, full = lax.optimization_barrier((packed, full))
    gathered = lax.all_gather(packed, WIDE_PARTS, axis=0, tiled=True)
    ids = gathered[:, twice_width].astype(jnp.int32)
    gathered = gathered[:, :twice_width]
    trail_id = ids - twice_width
    key = (trail_id // (trail_rows * col_count)) * trail_rows + trail_id % trail_rows
    _, order = lax.sort((key, jnp.arange(key.shape[0], dtype=jnp.int32)), num_keys=1)
    trail_src = order

    block_of = trail_id // BLOCK
    block_hits = (block_of[:, None] == jnp.arange(blocks)[None, :]).astype(jnp.int32)
    first_keep = jnp.sum(block_hits * fill_pattern[0][None, :], axis=1).astype(jnp.float32)
    second_keep = jnp.sum(block_hits * fill_pattern[1][None, :], axis=1).astype(jnp.float32)

    own_src = lax.dynamic_slice_in_dim(trail_src, wide_index * trail_rows, trail_rows, 0)
    column_first = jnp.arange(twice_width) < half_width
    own_keep = jnp.where(column_first[None, :], first_keep[own_src][:, None], second_keep[own_src][:, None])
    masked_own = gathered[own_src] * own_keep
    def exchange(tied):
        own, first, second, source = tied
        rows = own.shape[0]
        owners = jnp.zeros((col_count * rows, own.shape[1]), jnp.float32)
        owners = lax.dynamic_update_slice_in_dim(owners, own, col_index * rows, 0)
        for shift in range(1, col_count):
            pairs = [(c, (c + shift) % col_count) for c in range(col_count)]
            arrived = lax.ppermute(own, "col", pairs)
            owners = lax.dynamic_update_slice_in_dim(
                owners, arrived, ((col_index - shift) % col_count) * rows, 0)
        return (owners, first, second, source)

    factor, inverse, tied = factor_and_inverse(full, (masked_own, first_keep, second_keep, trail_src), exchange)
    masked_range, first_keep, second_keep, trail_src = tied
    range_panel = contract_rows(masked_range, inverse)
    panel = lax.dynamic_slice_in_dim(range_panel, col_index * trail_rows, trail_rows, 0)
    range_back = lax.dot_general(range_panel, inverse, (((1,), (0,)), ((), ())), precision=lax.Precision.HIGH)
    first_part = lax.dot_general(gathered[:, :half_width], range_back[:, :half_width],
                                 (((1,), (1,)), ((), ())), precision=lax.Precision.HIGH)
    second_part = lax.dot_general(gathered[:, half_width:], range_back[:, half_width:],
                                  (((1,), (1,)), ((), ())), precision=lax.Precision.HIGH)
    update_all = first_keep[:, None] * first_part + second_keep[:, None] * second_part
    update = update_all[trail_src]
    schur = trailing_block - update.reshape(trailing_block.shape)
    factor_rows = lax.dynamic_slice_in_dim(factor, device_index * diag_share, diag_share, 0)
    return (schur, panel, factor_rows)


def solution(mesh):
    wide_sizes = (4, 8, 2)
    split = jax.sharding.Mesh(
        mesh.devices.reshape(wide_sizes + (mesh.shape["col"],)), WIDE_PARTS + ("col",))
    rows = WIDE_PARTS + ("col",)
    in_specs = (P(rows, None), P(rows), P(), P(None, "col", None, WIDE_PARTS))
    out_specs = (P(None, "col", None, WIDE_PARTS), P(rows, None), P(rows, None))
    return jax.shard_map(local, mesh=split, in_specs=in_specs, out_specs=out_specs, check_vma=False)
```

```python
import jax
import jax.numpy as jnp
from jax import lax
from jax.sharding import PartitionSpec as P

BLOCK = 256
LANE_PAD = 128
WIDE_PARTS = ("y", "z", "core")
FACTOR_BLOCK = 128

highest = lax.Precision.HIGHEST


def lower_inverse(lower_factor):
    order_size = lower_factor.shape[0]
    identity = jnp.eye(order_size, dtype=lower_factor.dtype)
    return lax.linalg.triangular_solve(lower_factor, identity, left_side=True, lower=True)


def contract_rows(left_rows, right_rows):
    return lax.dot_general(left_rows, right_rows, (((1,), (1,)), ((), ())), precision=highest)


def matmul(left, right):
    return lax.dot_general(left, right, (((1,), (0,)), ((), ())), precision=highest)


def factor_and_inverse(gathered, tied, exchange):
    order_size = gathered.shape[0]
    size = FACTOR_BLOCK
    count = order_size // size
    factor = jnp.zeros((order_size, order_size), jnp.float32)
    diag_inverses = []
    for k in range(count):
        start = k * size
        column = (gathered[start:, start:start + size] + gathered[start:start + size, start:].T) * 0.5
        if k > 0:
            column = column - contract_rows(factor[start:, :start], factor[start:start + size, :start])
        block = jnp.tril(lax.linalg.cholesky(column[:size], symmetrize_input=False))
        block_inverse = jnp.tril(lower_inverse(block))
        factor = factor.at[start:start + size, start:start + size].set(block)
        if k < count - 1:
            factor = factor.at[start + size:, start:start + size].set(contract_rows(column[size:], block_inverse))
        diag_inverses.append(block_inverse)
        if k == count // 2:
            factor, tied = lax.optimization_barrier((factor, tied))
            tied = exchange(tied)
    inverse = jnp.zeros((order_size, order_size), jnp.float32)
    inverse = inverse.at[:size, :size].set(diag_inverses[0])
    for k in range(1, count):
        start = k * size
        partial = matmul(factor[start:start + size, :start], inverse[:start, :start])
        inverse = inverse.at[start:start + size, :start].set(-matmul(diag_inverses[k], partial))
        inverse = inverse.at[start:start + size, start:start + size].set(diag_inverses[k])
    return factor, inverse, tied


def local(assembled, row_map, fill_pattern, trailing_block):
    wide_count = lax.axis_size(WIDE_PARTS)
    col_count = lax.axis_size("col")
    asm_rows, twice_width = assembled.shape
    half_width = twice_width // 2
    trail_rows = trailing_block.shape[2]
    blocks = fill_pattern.shape[1]
    diag_share = twice_width // (col_count * wide_count)
    diag_col = twice_width // col_count
    trail_col = wide_count * trail_rows
    wide_index = lax.axis_index(WIDE_PARTS)
    col_index = lax.axis_index("col")
    device_index = wide_index * col_count + col_index
    is_diagonal = row_map < twice_width

    order_ids = jnp.argsort(jnp.where(is_diagonal, 0, 1), stable=True)[:diag_share]
    diag_ids = row_map[order_ids].astype(jnp.float32)
    diag_pack = jnp.concatenate(
        [assembled[order_ids], jnp.broadcast_to(diag_ids[:, None], (diag_share, LANE_PAD))], axis=1)
    for axis in (("y", "col"), ("z", "core")):
        diag_pack = lax.all_gather(diag_pack, axis, axis=0, tiled=True)
    diag_slot = diag_pack[:, twice_width].astype(jnp.int32)
    full = jnp.zeros((twice_width, twice_width), jnp.float32).at[diag_slot].set(
        diag_pack[:, :twice_width], mode="drop")

    trail_order = jnp.argsort(jnp.where(is_diagonal, 1, 0), stable=True)[:asm_rows - diag_share]
    trail_ids = row_map[trail_order]
    packed = jnp.concatenate(
        [assembled[trail_order],
         jnp.broadcast_to(trail_ids.astype(jnp.float32)[:, None], (asm_rows - diag_share, LANE_PAD))], axis=1)
    packed, full = lax.optimization_barrier((packed, full))
    gathered = lax.all_gather(packed, WIDE_PARTS, axis=0, tiled=True)
    ids = gathered[:, twice_width].astype(jnp.int32)
    gathered = gathered[:, :twice_width]
    trail_id = ids - twice_width
    key = (trail_id // (trail_rows * col_count)) * trail_rows + trail_id % trail_rows
    _, order = lax.sort((key, jnp.arange(key.shape[0], dtype=jnp.int32)), num_keys=1)
    trail_src = order

    block_of = trail_id // BLOCK
    block_hits = (block_of[:, None] == jnp.arange(blocks)[None, :]).astype(jnp.int32)
    first_keep = jnp.sum(block_hits * fill_pattern[0][None, :], axis=1).astype(jnp.float32)
    second_keep = jnp.sum(block_hits * fill_pattern[1][None, :], axis=1).astype(jnp.float32)

    own_src = lax.dynamic_slice_in_dim(trail_src, wide_index * trail_rows, trail_rows, 0)
    column_first = jnp.arange(twice_width) < half_width
    own_keep = jnp.where(column_first[None, :], first_keep[own_src][:, None], second_keep[own_src][:, None])
    masked_own = gathered[own_src] * own_keep
    def exchange(tied):
        own, first, second, source = tied
        rows = own.shape[0]
        owners = jnp.zeros((col_count * rows, own.shape[1]), jnp.float32)
        owners = lax.dynamic_update_slice_in_dim(owners, own, col_index * rows, 0)
        for shift in range(1, col_count):
            pairs = [(c, (c + shift) % col_count) for c in range(col_count)]
            arrived = lax.ppermute(own, "col", pairs)
            owners = lax.dynamic_update_slice_in_dim(
                owners, arrived, ((col_index - shift) % col_count) * rows, 0)
        return (owners, first, second, source)

    factor, inverse, tied = factor_and_inverse(full, (masked_own, first_keep, second_keep, trail_src), exchange)
    masked_range, first_keep, second_keep, trail_src = tied
    range_panel = contract_rows(masked_range, inverse)
    panel = lax.dynamic_slice_in_dim(range_panel, col_index * trail_rows, trail_rows, 0)
    range_back = lax.dot_general(range_panel, inverse, (((1,), (0,)), ((), ())), precision=lax.Precision.HIGH)
    first_part = lax.dot_general(gathered[:, :half_width], range_back[:, :half_width],
                                 (((1,), (1,)), ((), ())), precision=lax.Precision.HIGH)
    second_part = lax.dot_general(gathered[:, half_width:], range_back[:, half_width:],
                                  (((1,), (1,)), ((), ())), precision=lax.Precision.HIGH)
    update_all = first_keep[:, None] * first_part + second_keep[:, None] * second_part
    update = update_all[trail_src]
    schur = trailing_block - update.reshape(trailing_block.shape)
    factor_rows = lax.dynamic_slice_in_dim(factor, device_index * diag_share, diag_share, 0)
    return (schur, panel, factor_rows)


def solution(mesh):
    wide_sizes = (4, 8, 2)
    split = jax.sharding.Mesh(
        mesh.devices.reshape(wide_sizes + (mesh.shape["col"],)), WIDE_PARTS + ("col",))
    rows = WIDE_PARTS + ("col",)
    in_specs = (P(rows, None), P(rows), P(), P(None, "col", None, WIDE_PARTS))
    out_specs = (P(None, "col", None, WIDE_PARTS), P(rows, None), P(rows, None))
    return jax.shard_map(local, mesh=split, in_specs=in_specs, out_specs=out_specs, check_vma=False)
```

```python
import jax
import jax.numpy as jnp
from jax import lax
from jax.sharding import PartitionSpec as P

BLOCK = 256
LANE_PAD = 128
WIDE_PARTS = ("y", "z", "core")
FACTOR_BLOCK = 128

highest = lax.Precision.HIGHEST


def lower_inverse(lower_factor):
    order_size = lower_factor.shape[0]
    identity = jnp.eye(order_size, dtype=lower_factor.dtype)
    return lax.linalg.triangular_solve(lower_factor, identity, left_side=True, lower=True)


def contract_rows(left_rows, right_rows):
    return lax.dot_general(left_rows, right_rows, (((1,), (1,)), ((), ())), precision=highest)


def matmul(left, right):
    return lax.dot_general(left, right, (((1,), (0,)), ((), ())), precision=highest)


def factor_and_inverse(gathered, tied, exchange):
    order_size = gathered.shape[0]
    size = FACTOR_BLOCK
    count = order_size // size
    factor = jnp.zeros((order_size, order_size), jnp.float32)
    diag_inverses = []
    for k in range(count):
        start = k * size
        column = (gathered[start:, start:start + size] + gathered[start:start + size, start:].T) * 0.5
        if k > 0:
            column = column - contract_rows(factor[start:, :start], factor[start:start + size, :start])
        block = jnp.tril(lax.linalg.cholesky(column[:size], symmetrize_input=False))
        block_inverse = jnp.tril(lower_inverse(block))
        factor = factor.at[start:start + size, start:start + size].set(block)
        if k < count - 1:
            factor = factor.at[start + size:, start:start + size].set(contract_rows(column[size:], block_inverse))
        diag_inverses.append(block_inverse)
        if k == count // 2:
            factor, tied = lax.optimization_barrier((factor, tied))
            tied = exchange(tied)
    inverse = jnp.zeros((order_size, order_size), jnp.float32)
    inverse = inverse.at[:size, :size].set(diag_inverses[0])
    for k in range(1, count):
        start = k * size
        partial = matmul(factor[start:start + size, :start], inverse[:start, :start])
        inverse = inverse.at[start:start + size, :start].set(-matmul(diag_inverses[k], partial))
        inverse = inverse.at[start:start + size, start:start + size].set(diag_inverses[k])
    return factor, inverse, tied


def local(assembled, row_map, fill_pattern, trailing_block):
    wide_count = lax.axis_size(WIDE_PARTS)
    col_count = lax.axis_size("col")
    asm_rows, twice_width = assembled.shape
    half_width = twice_width // 2
    trail_rows = trailing_block.shape[2]
    blocks = fill_pattern.shape[1]
    diag_share = twice_width // (col_count * wide_count)
    diag_col = twice_width // col_count
    trail_col = wide_count * trail_rows
    wide_index = lax.axis_index(WIDE_PARTS)
    col_index = lax.axis_index("col")
    device_index = wide_index * col_count + col_index
    is_diagonal = row_map < twice_width

    order_ids = jnp.argsort(jnp.where(is_diagonal, 0, 1), stable=True)[:diag_share]
    diag_ids = row_map[order_ids].astype(jnp.float32)
    diag_pack = jnp.concatenate(
        [assembled[order_ids], jnp.broadcast_to(diag_ids[:, None], (diag_share, LANE_PAD))], axis=1)
    for axis in (("y", "col"), ("z", "core")):
        diag_pack = lax.all_gather(diag_pack, axis, axis=0, tiled=True)
    diag_slot = diag_pack[:, twice_width].astype(jnp.int32)
    full = jnp.zeros((twice_width, twice_width), jnp.float32).at[diag_slot].set(
        diag_pack[:, :twice_width], mode="drop")

    trail_order = jnp.argsort(jnp.where(is_diagonal, 1, 0), stable=True)[:asm_rows - diag_share]
    trail_ids = row_map[trail_order]
    packed = jnp.concatenate(
        [assembled[trail_order],
         jnp.broadcast_to(trail_ids.astype(jnp.float32)[:, None], (asm_rows - diag_share, LANE_PAD))], axis=1)
    packed, full = lax.optimization_barrier((packed, full))
    gathered = lax.all_gather(packed, WIDE_PARTS, axis=0, tiled=True)
    ids = gathered[:, twice_width].astype(jnp.int32)
    gathered = gathered[:, :twice_width]
    trail_id = ids - twice_width
    key = (trail_id // (trail_rows * col_count)) * trail_rows + trail_id % trail_rows
    _, order = lax.sort((key, jnp.arange(key.shape[0], dtype=jnp.int32)), num_keys=1)
    trail_src = order

    block_of = trail_id // BLOCK
    block_hits = (block_of[:, None] == jnp.arange(blocks)[None, :]).astype(jnp.int32)
    first_keep = jnp.sum(block_hits * fill_pattern[0][None, :], axis=1).astype(jnp.float32)
    second_keep = jnp.sum(block_hits * fill_pattern[1][None, :], axis=1).astype(jnp.float32)

    own_src = lax.dynamic_slice_in_dim(trail_src, wide_index * trail_rows, trail_rows, 0)
    column_first = jnp.arange(twice_width) < half_width
    own_keep = jnp.where(column_first[None, :], first_keep[own_src][:, None], second_keep[own_src][:, None])
    masked_own = gathered[own_src] * own_keep
    def exchange(tied):
        own, first, second, source = tied
        rows = own.shape[0]
        held = own
        shift = 1
        while shift < col_count:
            pairs = [(c, (c + shift) % col_count) for c in range(col_count)]
            held = jnp.concatenate([held, lax.ppermute(held, "col", pairs)], axis=0)
            shift *= 2
        owners = jnp.zeros((col_count * rows, own.shape[1]), jnp.float32)
        for back in range(col_count):
            owners = lax.dynamic_update_slice_in_dim(
                owners, held[back * rows:(back + 1) * rows], ((col_index - back) % col_count) * rows, 0)
        return (owners, first, second, source)

    factor, inverse, tied = factor_and_inverse(full, (masked_own, first_keep, second_keep, trail_src), exchange)
    masked_range, first_keep, second_keep, trail_src = tied
    range_panel = contract_rows(masked_range, inverse)
    panel = lax.dynamic_slice_in_dim(range_panel, col_index * trail_rows, trail_rows, 0)
    range_back = lax.dot_general(range_panel, inverse, (((1,), (0,)), ((), ())), precision=lax.Precision.HIGH)
    first_part = lax.dot_general(gathered[:, :half_width], range_back[:, :half_width],
                                 (((1,), (1,)), ((), ())), precision=lax.Precision.HIGH)
    second_part = lax.dot_general(gathered[:, half_width:], range_back[:, half_width:],
                                  (((1,), (1,)), ((), ())), precision=lax.Precision.HIGH)
    update_all = first_keep[:, None] * first_part + second_keep[:, None] * second_part
    update = update_all[trail_src]
    schur = trailing_block - update.reshape(trailing_block.shape)
    factor_rows = lax.dynamic_slice_in_dim(factor, device_index * diag_share, diag_share, 0)
    return (schur, panel, factor_rows)


def solution(mesh):
    wide_sizes = (4, 8, 2)
    split = jax.sharding.Mesh(
        mesh.devices.reshape(wide_sizes + (mesh.shape["col"],)), WIDE_PARTS + ("col",))
    rows = WIDE_PARTS + ("col",)
    in_specs = (P(rows, None), P(rows), P(), P(None, "col", None, WIDE_PARTS))
    out_specs = (P(None, "col", None, WIDE_PARTS), P(rows, None), P(rows, None))
    return jax.shard_map(local, mesh=split, in_specs=in_specs, out_specs=out_specs, check_vma=False)
```

```python
import jax
import jax.numpy as jnp
from jax import lax
from jax.sharding import PartitionSpec as P

BLOCK = 256
LANE_PAD = 128
WIDE_PARTS = ("y", "z", "core")
FACTOR_BLOCK = 128

highest = lax.Precision.HIGHEST


def lower_inverse(lower_factor):
    order_size = lower_factor.shape[0]
    identity = jnp.eye(order_size, dtype=lower_factor.dtype)
    return lax.linalg.triangular_solve(lower_factor, identity, left_side=True, lower=True)


def contract_rows(left_rows, right_rows):
    return lax.dot_general(left_rows, right_rows, (((1,), (1,)), ((), ())), precision=highest)


def matmul(left, right):
    return lax.dot_general(left, right, (((1,), (0,)), ((), ())), precision=highest)


def factor_and_inverse(gathered, tied, exchange):
    order_size = gathered.shape[0]
    size = FACTOR_BLOCK
    count = order_size // size
    factor = jnp.zeros((order_size, order_size), jnp.float32)
    diag_inverses = []
    for k in range(count):
        start = k * size
        column = (gathered[start:, start:start + size] + gathered[start:start + size, start:].T) * 0.5
        if k > 0:
            column = column - contract_rows(factor[start:, :start], factor[start:start + size, :start])
        block = jnp.tril(lax.linalg.cholesky(column[:size], symmetrize_input=False))
        block_inverse = jnp.tril(lower_inverse(block))
        factor = factor.at[start:start + size, start:start + size].set(block)
        if k < count - 1:
            factor = factor.at[start + size:, start:start + size].set(contract_rows(column[size:], block_inverse))
        diag_inverses.append(block_inverse)
        if k == count // 2:
            factor, tied = lax.optimization_barrier((factor, tied))
            tied = exchange(tied)
    inverse = jnp.zeros((order_size, order_size), jnp.float32)
    inverse = inverse.at[:size, :size].set(diag_inverses[0])
    for k in range(1, count):
        start = k * size
        partial = matmul(factor[start:start + size, :start], inverse[:start, :start])
        inverse = inverse.at[start:start + size, :start].set(-matmul(diag_inverses[k], partial))
        inverse = inverse.at[start:start + size, start:start + size].set(diag_inverses[k])
    return factor, inverse, tied


def local(assembled, row_map, fill_pattern, trailing_block):
    wide_count = lax.axis_size(WIDE_PARTS)
    col_count = lax.axis_size("col")
    asm_rows, twice_width = assembled.shape
    half_width = twice_width // 2
    trail_rows = trailing_block.shape[2]
    blocks = fill_pattern.shape[1]
    diag_share = twice_width // (col_count * wide_count)
    diag_col = twice_width // col_count
    trail_col = wide_count * trail_rows
    wide_index = lax.axis_index(WIDE_PARTS)
    col_index = lax.axis_index("col")
    device_index = wide_index * col_count + col_index
    is_diagonal = row_map < twice_width

    order_ids = jnp.argsort(jnp.where(is_diagonal, 0, 1), stable=True)[:diag_share]
    diag_ids = row_map[order_ids].astype(jnp.float32)
    diag_pack = jnp.concatenate(
        [assembled[order_ids], jnp.broadcast_to(diag_ids[:, None], (diag_share, LANE_PAD))], axis=1)
    for axis in (("y", "col", "core"), ("z",)):
        diag_pack = lax.all_gather(diag_pack, axis, axis=0, tiled=True)
    diag_slot = diag_pack[:, twice_width].astype(jnp.int32)
    full = jnp.zeros((twice_width, twice_width), jnp.float32).at[diag_slot].set(
        diag_pack[:, :twice_width], mode="drop")

    trail_order = jnp.argsort(jnp.where(is_diagonal, 1, 0), stable=True)[:asm_rows - diag_share]
    trail_ids = row_map[trail_order]
    packed = jnp.concatenate(
        [assembled[trail_order],
         jnp.broadcast_to(trail_ids.astype(jnp.float32)[:, None], (asm_rows - diag_share, LANE_PAD))], axis=1)
    packed, full = lax.optimization_barrier((packed, full))
    gathered = lax.all_gather(packed, WIDE_PARTS, axis=0, tiled=True)
    ids = gathered[:, twice_width].astype(jnp.int32)
    gathered = gathered[:, :twice_width]
    trail_id = ids - twice_width
    key = (trail_id // (trail_rows * col_count)) * trail_rows + trail_id % trail_rows
    _, order = lax.sort((key, jnp.arange(key.shape[0], dtype=jnp.int32)), num_keys=1)
    trail_src = order

    block_of = trail_id // BLOCK
    block_hits = (block_of[:, None] == jnp.arange(blocks)[None, :]).astype(jnp.int32)
    first_keep = jnp.sum(block_hits * fill_pattern[0][None, :], axis=1).astype(jnp.float32)
    second_keep = jnp.sum(block_hits * fill_pattern[1][None, :], axis=1).astype(jnp.float32)

    own_src = lax.dynamic_slice_in_dim(trail_src, wide_index * trail_rows, trail_rows, 0)
    column_first = jnp.arange(twice_width) < half_width
    own_keep = jnp.where(column_first[None, :], first_keep[own_src][:, None], second_keep[own_src][:, None])
    masked_own = gathered[own_src] * own_keep
    def exchange(tied):
        own, first, second, source = tied
        rows = own.shape[0]
        owners = jnp.zeros((col_count * rows, own.shape[1]), jnp.float32)
        owners = lax.dynamic_update_slice_in_dim(owners, own, col_index * rows, 0)
        for shift in range(1, col_count):
            pairs = [(c, (c + shift) % col_count) for c in range(col_count)]
            arrived = lax.ppermute(own, "col", pairs)
            owners = lax.dynamic_update_slice_in_dim(
                owners, arrived, ((col_index - shift) % col_count) * rows, 0)
        return (owners, first, second, source)

    factor, inverse, tied = factor_and_inverse(full, (masked_own, first_keep, second_keep, trail_src), exchange)
    masked_range, first_keep, second_keep, trail_src = tied
    range_panel = contract_rows(masked_range, inverse)
    panel = lax.dynamic_slice_in_dim(range_panel, col_index * trail_rows, trail_rows, 0)
    range_back = lax.dot_general(range_panel, inverse, (((1,), (0,)), ((), ())), precision=lax.Precision.HIGH)
    first_part = lax.dot_general(gathered[:, :half_width], range_back[:, :half_width],
                                 (((1,), (1,)), ((), ())), precision=lax.Precision.HIGH)
    second_part = lax.dot_general(gathered[:, half_width:], range_back[:, half_width:],
                                  (((1,), (1,)), ((), ())), precision=lax.Precision.HIGH)
    update_all = first_keep[:, None] * first_part + second_keep[:, None] * second_part
    update = update_all[trail_src]
    schur = trailing_block - update.reshape(trailing_block.shape)
    factor_rows = lax.dynamic_slice_in_dim(factor, device_index * diag_share, diag_share, 0)
    return (schur, panel, factor_rows)


def solution(mesh):
    wide_sizes = (4, 8, 2)
    split = jax.sharding.Mesh(
        mesh.devices.reshape(wide_sizes + (mesh.shape["col"],)), WIDE_PARTS + ("col",))
    rows = WIDE_PARTS + ("col",)
    in_specs = (P(rows, None), P(rows), P(), P(None, "col", None, WIDE_PARTS))
    out_specs = (P(None, "col", None, WIDE_PARTS), P(rows, None), P(rows, None))
    return jax.shard_map(local, mesh=split, in_specs=in_specs, out_specs=out_specs, check_vma=False)
```
